768 devices in a mesh: segment: 4 (over x), mp: 96 (over z, y), seq: 2 (over core).
Axes of the slice: x: 4, y: 8, z: 12, core: 2. Of those that a mesh axis runs over, the one named last changes fastest.
Arguments:
- frames_in: bfloat16 [96, 8, 4, 24, 128], P('mp', 'segment', 'seq'), may hold values from -6 to 6
- valid_frames: int32 [96], P('mp'), may hold values from 1 to 4, as said below
- tokenizer_slot: int32 [96], P('mp'), may hold values from 0 to 95, as said below
- conv_w: bfloat16 [3, 128, 128], replicated, may hold values from -0.3125 to 0.3125
- embed_w: bfloat16 [128, 5120], P(None, 'seq'), may hold values from -0.5 to 0.5
- qkv_w: bfloat16 [5120, 20, 384], P('seq', 'segment'), may hold values from -0.078125 to 0.078125
- out_grad: bfloat16 [96, 4, 4, 24, 20, 128], P('mp', None, 'seq', None, 'segment'), may hold values from -6 to 6
Outputs:
- attn_out: bfloat16 [96, 4, 4, 24, 20, 128], P('mp', None, 'seq', None, 'segment')
- q_grad: bfloat16 [96, 4, 4, 24, 20, 128], P('mp', None, 'seq', None, 'segment')
- k_grad: bfloat16 [96, 4, 4, 24, 20, 128], P('mp', None, 'seq', None, 'segment')
- v_grad: bfloat16 [96, 4, 4, 24, 20, 128], P('mp', None, 'seq', None, 'segment')
The draws below stay inside these ranges and needn't reach their ends.
Inputs may be any that keep to these rules, and one draw needn't show every extreme that they name: valid_frames[b] counts the leading latent frames of clip b that hold video; some clip has all 4. `tokenizer_slot`: every tokenizer slot encodes exactly one clip; some clip b takes the slot (b + 48) modulo 96.
All inputs are finite; a program needn't handle non-finite values.
Results may differ from the reference program's by a relative error of at most 0.012.
Values may be sent and summed in bfloat16 or wider, within the bound.
No kernel may reach another device: no remote copies, remote signals or barrier semaphores. Data moves between devices by JAX's collectives and lax.ppermute only.
A program may use at most 32 MiB of HBM per device.

```python
import math
import jax
import jax.numpy as jnp
from jax import lax

CT = 128
D = 5120
HS = 128
HEADS = 20
COLS = 24
MB = 96
LATF = 4
FRAMES = 8
ROWS = 4


def draw_valid_frames(key, part):
    first, second = jax.random.split(jax.random.fold_in(key, 11))
    counts = jax.random.randint(first, (MB,), 1, LATF + 1)
    full_at = jax.random.randint(second, (), 0, MB)
    return jnp.where(jnp.arange(MB) == full_at, LATF, counts).astype(jnp.int32)


def draw_tokenizer_slot(key, part):
    first, second = jax.random.split(jax.random.fold_in(key, 23))
    order = jax.random.permutation(first, MB).astype(jnp.int32)
    chosen = jax.random.randint(second, (), 0, MB).astype(jnp.int32)
    target = (chosen + MB // 2) % MB
    places = jnp.arange(MB, dtype=jnp.int32)
    where_target = jnp.sum(jnp.where(order == target, places, 0)).astype(jnp.int32)
    previous = jnp.sum(jnp.where(places == chosen, order, 0)).astype(jnp.int32)
    order = jnp.where(places == where_target, previous, order)
    order = jnp.where(places == chosen, target, order)
    return order.astype(jnp.int32)


def block_scale(own_key, shape, pieces, smallest, high):
    level, own = 1.0, jax.random.fold_in(own_key, 6)
    for dim, blocks in pieces:
        draws = jnp.exp(jax.random.uniform(jax.random.fold_in(own, dim), (blocks,), jnp.float32, smallest / len(pieces), high / len(pieces)))
        level = level * jnp.repeat(draws, shape[dim] // blocks).reshape([-1 if axis == dim else 1 for axis in range(len(shape))])
    return level


def centred(key, dims, spread, most, shards=(), kind=jnp.bfloat16):
    result = spread * jax.random.normal(key, dims, jnp.float32)
    if shards:
        result = result * block_scale(key, dims, shards, -0.22, 0.18)
    return jnp.clip(result, -most, most).astype(kind)


def setup_inputs(seed: int = 0) -> dict:
    key_list = jax.random.split(jax.random.key(seed), 8)
    return {
        "frames_in": centred(key_list[0], (MB, FRAMES, ROWS, COLS, CT), 1.0, 6.0, ((0, 96), (1, 4), (2, 2))),
        "valid_frames": draw_valid_frames(jax.random.fold_in(key_list[7], 71), 0),
        "tokenizer_slot": draw_tokenizer_slot(jax.random.fold_in(key_list[7], 71), 0),
        "conv_w": centred(key_list[3], (3, CT, CT), (3 * CT) ** -0.5, 0.3125),
        "embed_w": centred(key_list[4], (CT, D), CT ** -0.5, 0.5, ((1, 2),)),
        "qkv_w": centred(key_list[5], (D, HEADS, 3 * HS), D ** -0.5, 0.078125, ((0, 2), (1, 4))),
        "out_grad": centred(key_list[6], (MB, LATF, ROWS, COLS, HEADS, HS), 1.0, 6.0, ((0, 96), (2, 2), (4, 4))),
    }


def attend(queries, keys, values, keep, grad):
    scale = 1.0 / math.sqrt(queries.shape[-1])
    scores = jnp.einsum('qhd,khd->hqk', queries.astype(jnp.float32), keys.astype(jnp.float32)) * scale
    scores = jnp.where(keep[None, None, :], scores, -jnp.inf)
    top = lax.optimization_barrier(jnp.max(scores, axis=-1, keepdims=True))
    lse = top + jnp.log(lax.optimization_barrier(jnp.sum(jnp.exp(scores - top), axis=-1, keepdims=True)))
    prob = jnp.exp(scores - lse)
    prob_b = prob.astype(jnp.bfloat16)
    attn = jnp.einsum('hqk,khd->qhd', prob_b.astype(jnp.float32), values.astype(jnp.float32)).astype(jnp.bfloat16)
    dprob = jnp.einsum('qhd,khd->hqk', grad.astype(jnp.float32), values.astype(jnp.float32))
    delta = lax.optimization_barrier(jnp.sum(grad.astype(jnp.float32) * attn.astype(jnp.float32), axis=-1)).T
    dscore = (prob * (dprob - delta[:, :, None])).astype(jnp.bfloat16)
    q_grad = (jnp.einsum('hqk,khd->qhd', dscore.astype(jnp.float32), keys.astype(jnp.float32)) * scale).astype(jnp.bfloat16)
    k_grad = (jnp.einsum('hqk,qhd->khd', dscore.astype(jnp.float32), queries.astype(jnp.float32)) * scale).astype(jnp.bfloat16)
    v_grad = jnp.einsum('hqk,qhd->khd', prob_b.astype(jnp.float32), grad.astype(jnp.float32)).astype(jnp.bfloat16)
    return (attn, q_grad, k_grad, v_grad)

def reference(frames_in, valid_frames, tokenizer_slot, conv_w, embed_w, qkv_w, out_grad):
    wide = frames_in.astype(jnp.float32)
    taps = conv_w.astype(jnp.float32)
    current = wide[:, 1::2]
    middle = wide[:, 0::2]
    earlier = jnp.concatenate([jnp.zeros_like(wide[:, :1]), wide[:, 1::2][:, :-1]], axis=1)
    conv = jnp.einsum('bfrcx,xy->bfrcy', current, taps[0])
    conv = conv + jnp.einsum('bfrcx,xy->bfrcy', middle, taps[1])
    conv = conv + jnp.einsum('bfrcx,xy->bfrcy', earlier, taps[2])
    act = jax.nn.silu(conv).astype(jnp.bfloat16)
    clip_act = jnp.take(act, tokenizer_slot.astype(jnp.int32), axis=0)
    weights = qkv_w.reshape(D, HEADS * 3 * HS)

    def one_clip(pack):
        clip, limit, grad = pack
        shape = clip.shape
        tokens = shape[0] * shape[1] * shape[2]
        hidden = jnp.dot(clip.reshape(tokens, CT), embed_w, preferred_element_type=jnp.float32).astype(jnp.bfloat16)
        qkv = jnp.dot(hidden, weights, preferred_element_type=jnp.float32).astype(jnp.bfloat16)
        qkv = qkv.reshape(tokens, HEADS, 3 * HS)
        queries = qkv[..., :HS]
        keys = qkv[..., HS:2 * HS]
        values = qkv[..., 2 * HS:]
        frame_of = jnp.arange(tokens, dtype=jnp.int32) // (shape[1] * shape[2])
        keep = frame_of < limit
        results = attend(queries, keys, values, keep, grad.reshape(tokens, HEADS, HS))
        return tuple((item.reshape(shape[0], shape[1], shape[2], HEADS, HS) for item in results))
    attn_out, q_grad, k_grad, v_grad = lax.map(one_clip, (clip_act, valid_frames, out_grad))
    return (attn_out, q_grad, k_grad, v_grad)
```

```python
import math

import jax
import jax.numpy as jnp
import numpy as np
from jax import lax
from jax.sharding import Mesh
from jax.sharding import PartitionSpec as P

OUTER = "mp_outer"
INNER = "mp_inner"
MP = (OUTER, INNER)


def passed_along(shard, axis, by):
    count = lax.axis_size(axis)
    pairs = [(i, i + by) for i in range(count) if 0 <= i + by < count]
    return lax.ppermute(shard, axis, pairs)


def swap_seq(x):
    return lax.ppermute(x, "seq", [(0, 1), (1, 0)])


def causal_conv(frames, conv_w):
    earlier = passed_along(frames[1:2], "segment", 1)[0]
    total = jnp.einsum("rcx,xy->rcy", frames[1], conv_w[0], preferred_element_type=jnp.float32)
    total = total + jnp.einsum(
        "rcx,xy->rcy", frames[0], conv_w[1], preferred_element_type=jnp.float32
    )
    total = total + jnp.einsum(
        "rcx,xy->rcy", earlier, conv_w[2], preferred_element_type=jnp.float32
    )
    return jax.nn.silu(total).astype(jnp.bfloat16)


def route(act, tokenizer_slot):
    n_in = lax.axis_size(INNER)
    n_out = lax.axis_size(OUTER)
    my_out = lax.axis_index(OUTER)
    source = tokenizer_slot[0]
    row = lax.all_gather(act, INNER, axis=0)
    wanted = lax.all_gather(tokenizer_slot, OUTER, axis=0, tiled=True)
    pick = jnp.clip(wanted % n_in, 0, n_in - 1)
    mine = (wanted // n_in) == my_out
    send = jnp.take(row, pick, axis=0)
    send = jnp.where(mine.reshape((n_out,) + (1,) * act.ndim), send, jnp.zeros_like(send))
    got = lax.all_to_all(send, OUTER, 0, 0, tiled=True)
    origin = jnp.clip(source // n_in, 0, n_out - 1)
    return lax.dynamic_index_in_dim(got, origin, 0, keepdims=False)


def masked_scores(queries, keys, keep, scale):
    scores = jnp.einsum("qhd,khd->hqk", queries, keys, preferred_element_type=jnp.float32) * scale
    return jnp.where(keep[None, None, :], scores, -jnp.inf)


def on_device(frames_in, valid_frames, tokenizer_slot, conv_w, embed_w, qkv_w, out_grad):
    act = causal_conv(frames_in[0], conv_w)
    row_dev, cols, channels = act.shape
    routed = route(act, tokenizer_slot)
    latent = lax.all_gather(routed[None], ("segment", "seq"), axis=0, tiled=True)
    n_seg = lax.axis_size("segment")
    n_seq = lax.axis_size("seq")
    latent = latent.reshape(n_seg, n_seq * row_dev, cols, channels)
    hidden = jnp.einsum(
        "frcx,xd->frcd", latent, embed_w, preferred_element_type=jnp.float32
    ).astype(jnp.bfloat16)
    partial_qkv = jnp.einsum("frcd,dhe->frche", hidden, qkv_w, preferred_element_type=jnp.float32)
    heads_local = qkv_w.shape[1]
    head_size = qkv_w.shape[2] // 3
    rows = n_seq * row_dev
    me = lax.axis_index("seq")
    other = 1 - me
    own_part = lax.dynamic_slice_in_dim(partial_qkv, me * row_dev, row_dev, 1)
    sent_part = lax.dynamic_slice_in_dim(partial_qkv, other * row_dev, row_dev, 1)
    own_qkv = (own_part + swap_seq(sent_part)).astype(jnp.bfloat16)
    own_pair = own_qkv[..., head_size:]
    other_pair = swap_seq(own_pair)
    all_pair = jnp.concatenate([own_pair, other_pair], axis=1)
    queries5 = own_qkv[..., :head_size]
    scale = 1.0 / math.sqrt(head_size)
    n_query = n_seg * row_dev * cols
    n_key = n_seg * rows * cols
    q_flat = queries5.reshape(n_query, heads_local, head_size)
    keys = all_pair[..., :head_size].reshape(n_key, heads_local, head_size)
    values = all_pair[..., head_size:].reshape(n_key, heads_local, head_size)
    limit = valid_frames[0]
    keep = jnp.arange(n_key, dtype=jnp.int32) // (rows * cols) < limit
    scores = masked_scores(q_flat, keys, keep, scale)
    top = jnp.max(scores, axis=-1, keepdims=True)
    lse = top + jnp.log(jnp.sum(jnp.exp(scores - top), axis=-1, keepdims=True))
    prob = jnp.exp(scores - lse)
    prob_b = prob.astype(jnp.bfloat16)
    attn = jnp.einsum("hqk,khd->qhd", prob_b, values, preferred_element_type=jnp.float32).astype(
        jnp.bfloat16
    )
    grad = out_grad.reshape(n_query, heads_local, head_size)
    dprob = jnp.einsum("qhd,khd->hqk", grad, values, preferred_element_type=jnp.float32)
    delta = jnp.sum(grad.astype(jnp.float32) * attn.astype(jnp.float32), axis=-1).T
    dscore = (prob * (dprob - delta[:, :, None])).astype(jnp.bfloat16)
    q_grad = (
        jnp.einsum("hqk,khd->qhd", dscore, keys, preferred_element_type=jnp.float32) * scale
    ).astype(jnp.bfloat16)
    key_part = (
        jnp.einsum("hqk,qhd->khd", dscore, q_flat, preferred_element_type=jnp.float32) * scale
    ).astype(jnp.bfloat16)
    value_part = jnp.einsum(
        "hqk,qhd->khd", prob_b, grad, preferred_element_type=jnp.float32
    ).astype(jnp.bfloat16)
    kv_part = jnp.stack([key_part, value_part]).reshape(
        2, n_seg, 2, row_dev, cols, heads_local, head_size
    )
    kv_sum = kv_part[:, :, 0].astype(jnp.float32) + swap_seq(kv_part[:, :, 1]).astype(jnp.float32)
    kv_sum = kv_sum.astype(jnp.bfloat16)
    k_grad = kv_sum[0]
    v_grad = kv_sum[1]
    shape6 = (1, n_seg, row_dev, cols, heads_local, head_size)
    return (
        attn.reshape(shape6),
        q_grad.reshape(shape6),
        k_grad.reshape(shape6),
        v_grad.reshape(shape6),
    )


def inner_size(mesh):
    column = np.asarray(mesh.devices)[0, :, 0]
    try:
        count = len({d.coords[1] for d in column})
    except AttributeError:
        count = 1
    if count < 1 or column.size % count:
        count = 1
    return count


def solution(mesh):
    devices = np.asarray(mesh.devices)
    n_seg, n_mp, n_seq = devices.shape
    n_in = inner_size(mesh)
    split = Mesh(
        devices.reshape(n_seg, n_mp // n_in, n_in, n_seq), ("segment", OUTER, INNER, "seq")
    )
    placed = (
        P(MP, "segment", "seq", None, None),
        P(MP),
        P(MP),
        P(),
        P(None, "seq"),
        P("seq", "segment", None),
        P(MP, None, "seq", None, "segment", None),
    )
    out = P(MP, None, "seq", None, "segment", None)
    return jax.shard_map(
        on_device,
        mesh=split,
        in_specs=placed,
        out_specs=(out, out, out, out),
        check_vma=False,
    )
```

```python
import math

import jax
import jax.numpy as jnp
import numpy as np
from jax import lax
from jax.sharding import Mesh
from jax.sharding import PartitionSpec as P

OUTER = "mp_outer"
INNER = "mp_inner"
MP = (OUTER, INNER)


def passed_along(shard, axis, by):
    count = lax.axis_size(axis)
    pairs = [(i, i + by) for i in range(count) if 0 <= i + by < count]
    return lax.ppermute(shard, axis, pairs)


def swap_seq(x):
    return lax.ppermute(x, "seq", [(0, 1), (1, 0)])


def causal_conv(frames, conv_w):
    earlier = passed_along(frames[1:2], "segment", 1)[0]
    total = jnp.einsum("rcx,xy->rcy", frames[1], conv_w[0], preferred_element_type=jnp.float32)
    total = total + jnp.einsum(
        "rcx,xy->rcy", frames[0], conv_w[1], preferred_element_type=jnp.float32
    )
    total = total + jnp.einsum(
        "rcx,xy->rcy", earlier, conv_w[2], preferred_element_type=jnp.float32
    )
    return jax.nn.silu(total).astype(jnp.bfloat16)


def gather_rotated(x, axis):
    n = lax.axis_size(axis)
    have = x[None]
    shift = 1
    while have.shape[0] < n:
        need = min(have.shape[0], n - have.shape[0])
        pairs = [(j, (j - shift) % n) for j in range(n)]
        have = jnp.concatenate([have, lax.ppermute(have[:need], axis, pairs)], axis=0)
        shift *= 2
    return have


def gather_ordered(x, axis):
    n = lax.axis_size(axis)
    have = gather_rotated(x, axis)
    if n == 1:
        return have
    me = lax.axis_index(axis)
    return jnp.take(have, (jnp.arange(n) - me) % n, axis=0)


def route(act, tokenizer_slot):
    n_in = lax.axis_size(INNER)
    n_out = lax.axis_size(OUTER)
    my_out = lax.axis_index(OUTER)
    my_in = lax.axis_index(INNER)
    source = tokenizer_slot[0]
    row = gather_rotated(act, INNER)
    wanted = gather_ordered(tokenizer_slot, OUTER)[:, 0]
    pick = (wanted % n_in - my_in) % n_in
    mine = (wanted // n_in) == my_out
    send = jnp.take(row, pick, axis=0)
    send = jnp.where(mine.reshape((n_out,) + (1,) * act.ndim), send, jnp.zeros_like(send))
    got = lax.all_to_all(send, OUTER, 0, 0, tiled=True)
    origin = jnp.clip(source // n_in, 0, n_out - 1)
    return lax.dynamic_index_in_dim(got, origin, 0, keepdims=False)


def masked_scores(queries, keys, keep, scale):
    scores = jnp.einsum("qhd,khd->hqk", queries, keys, preferred_element_type=jnp.float32) * scale
    return jnp.where(keep[None, None, :], scores, -jnp.inf)


def on_device(frames_in, valid_frames, tokenizer_slot, conv_w, embed_w, qkv_w, out_grad):
    act = causal_conv(frames_in[0], conv_w)
    row_dev, cols, channels = act.shape
    routed = route(act, tokenizer_slot)
    n_seg = lax.axis_size("segment")
    n_seq = lax.axis_size("seq")
    pair = gather_rotated(routed, "seq")
    latent = gather_ordered(pair, "segment")
    heads_local = qkv_w.shape[1]
    head_size = qkv_w.shape[2] // 3
    rows = n_seq * row_dev

    def project(piece):
        hidden = jnp.einsum(
            "frcx,xd->frcd", piece, embed_w, preferred_element_type=jnp.float32
        ).astype(jnp.bfloat16)
        return jnp.einsum("frcd,dhe->frche", hidden, qkv_w, preferred_element_type=jnp.float32)

    received = swap_seq(project(latent[:, 1]))
    own_qkv = (project(latent[:, 0]) + received).astype(jnp.bfloat16)
    own_pair = own_qkv[..., head_size:]
    other_pair = swap_seq(own_pair)
    all_pair = jnp.concatenate([own_pair, other_pair], axis=1)
    queries5 = own_qkv[..., :head_size]
    scale = 1.0 / math.sqrt(head_size)
    n_query = n_seg * row_dev * cols
    n_key = n_seg * rows * cols
    q_flat = queries5.reshape(n_query, heads_local, head_size)
    keys = all_pair[..., :head_size].reshape(n_key, heads_local, head_size)
    values = all_pair[..., head_size:].reshape(n_key, heads_local, head_size)
    limit = valid_frames[0]
    keep = jnp.arange(n_key, dtype=jnp.int32) // (rows * cols) < limit
    scores = masked_scores(q_flat, keys, keep, scale)
    top = jnp.max(scores, axis=-1, keepdims=True)
    lse = top + jnp.log(jnp.sum(jnp.exp(scores - top), axis=-1, keepdims=True))
    prob = jnp.exp(scores - lse)
    prob_b = prob.astype(jnp.bfloat16)
    attn = jnp.einsum("hqk,khd->qhd", prob_b, values, preferred_element_type=jnp.float32).astype(
        jnp.bfloat16
    )
    grad = out_grad.reshape(n_query, heads_local, head_size)
    dprob = jnp.einsum("qhd,khd->hqk", grad, values, preferred_element_type=jnp.float32)
    delta = jnp.sum(grad.astype(jnp.float32) * attn.astype(jnp.float32), axis=-1).T
    dscore = (prob * (dprob - delta[:, :, None])).astype(jnp.bfloat16)
    q_grad = (
        jnp.einsum("hqk,khd->qhd", dscore, keys, preferred_element_type=jnp.float32) * scale
    ).astype(jnp.bfloat16)
    key_part = (
        jnp.einsum("hqk,qhd->khd", dscore, q_flat, preferred_element_type=jnp.float32) * scale
    ).astype(jnp.bfloat16)
    value_part = jnp.einsum(
        "hqk,qhd->khd", prob_b, grad, preferred_element_type=jnp.float32
    ).astype(jnp.bfloat16)
    kv_part = jnp.stack([key_part, value_part]).reshape(
        2, n_seg, 2, row_dev, cols, heads_local, head_size
    )
    kv_sum = kv_part[:, :, 0].astype(jnp.float32) + swap_seq(kv_part[:, :, 1]).astype(jnp.float32)
    kv_sum = kv_sum.astype(jnp.bfloat16)
    k_grad = kv_sum[0]
    v_grad = kv_sum[1]
    shape6 = (1, n_seg, row_dev, cols, heads_local, head_size)
    return (
        attn.reshape(shape6),
        q_grad.reshape(shape6),
        k_grad.reshape(shape6),
        v_grad.reshape(shape6),
    )


def inner_size(mesh):
    column = np.asarray(mesh.devices)[0, :, 0]
    try:
        count = len({d.coords[1] for d in column})
    except AttributeError:
        count = 1
    if count < 1 or column.size % count:
        count = 1
    return count


def solution(mesh):
    devices = np.asarray(mesh.devices)
    n_seg, n_mp, n_seq = devices.shape
    n_in = inner_size(mesh)
    split = Mesh(
        devices.reshape(n_seg, n_mp // n_in, n_in, n_seq), ("segment", OUTER, INNER, "seq")
    )
    placed = (
        P(MP, "segment", "seq", None, None),
        P(MP),
        P(MP),
        P(),
        P(None, "seq"),
        P("seq", "segment", None),
        P(MP, None, "seq", None, "segment", None),
    )
    out = P(MP, None, "seq", None, "segment", None)
    return jax.shard_map(
        on_device,
        mesh=split,
        in_specs=placed,
        out_specs=(out, out, out, out),
        check_vma=False,
    )
```

```python
import math

import jax
import jax.numpy as jnp
import numpy as np
from jax import lax
from jax.sharding import Mesh
from jax.sharding import PartitionSpec as P

OUTER = "mp_outer"
INNER = "mp_inner"
MP = (OUTER, INNER)
SLOT_MODE = 'a2a'
ROW_MODE = 'a2a'
FANOUT = 'a2a'
RAW = True


def passed_along(shard, axis, by):
    count = lax.axis_size(axis)
    pairs = [(i, i + by) for i in range(count) if 0 <= i + by < count]
    return lax.ppermute(shard, axis, pairs)


def swap_seq(x):
    return lax.ppermute(x, "seq", [(0, 1), (1, 0)])


def causal_conv(frames, conv_w):
    earlier = passed_along(frames[1:2], "segment", 1)[0]
    total = jnp.einsum("rcx,xy->rcy", frames[1], conv_w[0], preferred_element_type=jnp.float32)
    total = total + jnp.einsum(
        "rcx,xy->rcy", frames[0], conv_w[1], preferred_element_type=jnp.float32
    )
    total = total + jnp.einsum(
        "rcx,xy->rcy", earlier, conv_w[2], preferred_element_type=jnp.float32
    )
    return jax.nn.silu(total).astype(jnp.bfloat16)


def gather_rotated(x, axis):
    n = lax.axis_size(axis)
    have = x[None]
    shift = 1
    while have.shape[0] < n:
        need = min(have.shape[0], n - have.shape[0])
        pairs = [(j, (j - shift) % n) for j in range(n)]
        have = jnp.concatenate([have, lax.ppermute(have[:need], axis, pairs)], axis=0)
        shift *= 2
    return have


def gather_ordered(x, axis):
    n = lax.axis_size(axis)
    have = gather_rotated(x, axis)
    if n == 1:
        return have
    me = lax.axis_index(axis)
    return jnp.take(have, (jnp.arange(n) - me) % n, axis=0)


def gather_a2a(x, axis):
    n = lax.axis_size(axis)
    send = jnp.broadcast_to(x[None], (n,) + x.shape)
    return lax.all_to_all(send, axis, 0, 0, tiled=True)


def gather(x, axis, mode):
    if mode == "a2a":
        return gather_a2a(x, axis)
    if mode == "ag":
        return lax.all_gather(x, axis, axis=0)
    return gather_ordered(x, axis)


def route(piece, tokenizer_slot):
    n_in = lax.axis_size(INNER)
    n_out = lax.axis_size(OUTER)
    my_out = lax.axis_index(OUTER)
    source = tokenizer_slot[0]
    wanted = gather(tokenizer_slot, OUTER, SLOT_MODE)[:, 0]
    row = gather(piece, INNER, ROW_MODE)
    pick = jnp.clip(wanted % n_in, 0, n_in - 1)
    mine = (wanted // n_in) == my_out
    send = jnp.take(row, pick, axis=0)
    send = jnp.where(mine.reshape((n_out,) + (1,) * piece.ndim), send, jnp.zeros_like(send))
    origin = jnp.clip(source // n_in, 0, n_out - 1)
    if FANOUT == "merged":
        n_grp = lax.axis_size("segment") * lax.axis_size("seq")
        wide = jnp.broadcast_to(send[:, None], (n_out, n_grp) + piece.shape)
        wide = wide.reshape((n_out * n_grp,) + piece.shape)
        got = lax.all_to_all(wide, (OUTER, "segment", "seq"), 0, 0, tiled=True)
        got = got.reshape((n_out, n_grp) + piece.shape)
        return lax.dynamic_index_in_dim(got, origin, 0, keepdims=False)
    got = lax.all_to_all(send, OUTER, 0, 0, tiled=True)
    routed = lax.dynamic_index_in_dim(got, origin, 0, keepdims=False)
    return gather(routed, ("segment", "seq"), FANOUT)


def conv_all(frames, conv_w):
    current = frames[1::2]
    middle = frames[0::2]
    earlier = jnp.concatenate([jnp.zeros_like(current[:1]), current[:-1]], axis=0)
    total = jnp.einsum("frcx,xy->frcy", current, conv_w[0], preferred_element_type=jnp.float32)
    total = total + jnp.einsum(
        "frcx,xy->frcy", middle, conv_w[1], preferred_element_type=jnp.float32
    )
    total = total + jnp.einsum(
        "frcx,xy->frcy", earlier, conv_w[2], preferred_element_type=jnp.float32
    )
    return jax.nn.silu(total).astype(jnp.bfloat16)


def masked_scores(queries, keys, keep, scale):
    scores = jnp.einsum("qhd,khd->hqk", queries, keys, preferred_element_type=jnp.float32) * scale
    return jnp.where(keep[None, None, :], scores, -jnp.inf)


def on_device(frames_in, valid_frames, tokenizer_slot, conv_w, embed_w, qkv_w, out_grad):
    n_seg = lax.axis_size("segment")
    n_seq = lax.axis_size("seq")
    me = lax.axis_index("seq")
    if RAW:
        local = frames_in[0]
        n_fr, row_dev, cols, channels = local.shape
        pieces = route(local, tokenizer_slot).reshape(
            (n_seg, n_seq, n_fr, row_dev, cols, channels)
        )
        frames = pieces.transpose(0, 2, 1, 3, 4, 5).reshape(
            n_seg * n_fr, n_seq * row_dev, cols, channels
        )
        act_all = conv_all(frames, conv_w).reshape(n_seg, n_seq, row_dev, cols, channels)
    else:
        act = causal_conv(frames_in[0], conv_w)
        row_dev, cols, channels = act.shape
        act_all = route(act, tokenizer_slot).reshape(n_seg, n_seq, row_dev, cols, channels)
    own_rows = lax.dynamic_index_in_dim(act_all, me, 1, keepdims=False)
    other_rows = lax.dynamic_index_in_dim(act_all, 1 - me, 1, keepdims=False)
    latent = jnp.stack([own_rows, other_rows], axis=1)
    heads_local = qkv_w.shape[1]
    head_size = qkv_w.shape[2] // 3
    rows = n_seq * row_dev

    def project(piece):
        hidden = jnp.einsum(
            "frcx,xd->frcd", piece, embed_w, preferred_element_type=jnp.float32
        ).astype(jnp.bfloat16)
        return jnp.einsum("frcd,dhe->frche", hidden, qkv_w, preferred_element_type=jnp.float32)

    received = swap_seq(project(latent[:, 1]))
    own_qkv = (project(latent[:, 0]) + received).astype(jnp.bfloat16)
    own_pair = own_qkv[..., head_size:]
    other_pair = swap_seq(own_pair)
    all_pair = jnp.concatenate([own_pair, other_pair], axis=1)
    queries5 = own_qkv[..., :head_size]
    scale = 1.0 / math.sqrt(head_size)
    n_query = n_seg * row_dev * cols
    n_key = n_seg * rows * cols
    q_flat = queries5.reshape(n_query, heads_local, head_size)
    keys = all_pair[..., :head_size].reshape(n_key, heads_local, head_size)
    values = all_pair[..., head_size:].reshape(n_key, heads_local, head_size)
    limit = valid_frames[0]
    keep = jnp.arange(n_key, dtype=jnp.int32) // (rows * cols) < limit
    scores = masked_scores(q_flat, keys, keep, scale)
    top = jnp.max(scores, axis=-1, keepdims=True)
    lse = top + jnp.log(jnp.sum(jnp.exp(scores - top), axis=-1, keepdims=True))
    prob = jnp.exp(scores - lse)
    prob_b = prob.astype(jnp.bfloat16)
    attn = jnp.einsum("hqk,khd->qhd", prob_b, values, preferred_element_type=jnp.float32).astype(
        jnp.bfloat16
    )
    grad = out_grad.reshape(n_query, heads_local, head_size)
    dprob = jnp.einsum("qhd,khd->hqk", grad, values, preferred_element_type=jnp.float32)
    delta = jnp.sum(grad.astype(jnp.float32) * attn.astype(jnp.float32), axis=-1).T
    dscore = (prob * (dprob - delta[:, :, None])).astype(jnp.bfloat16)
    q_grad = (
        jnp.einsum("hqk,khd->qhd", dscore, keys, preferred_element_type=jnp.float32) * scale
    ).astype(jnp.bfloat16)
    key_part = (
        jnp.einsum("hqk,qhd->khd", dscore, q_flat, preferred_element_type=jnp.float32) * scale
    ).astype(jnp.bfloat16)
    value_part = jnp.einsum(
        "hqk,qhd->khd", prob_b, grad, preferred_element_type=jnp.float32
    ).astype(jnp.bfloat16)
    kv_part = jnp.stack([key_part, value_part]).reshape(
        2, n_seg, 2, row_dev, cols, heads_local, head_size
    )
    kv_sum = kv_part[:, :, 0].astype(jnp.float32) + swap_seq(kv_part[:, :, 1]).astype(jnp.float32)
    kv_sum = kv_sum.astype(jnp.bfloat16)
    k_grad = kv_sum[0]
    v_grad = kv_sum[1]
    shape6 = (1, n_seg, row_dev, cols, heads_local, head_size)
    return (
        attn.reshape(shape6),
        q_grad.reshape(shape6),
        k_grad.reshape(shape6),
        v_grad.reshape(shape6),
    )


def inner_size(mesh):
    column = np.asarray(mesh.devices)[0, :, 0]
    try:
        count = len({d.coords[1] for d in column})
    except AttributeError:
        count = 1
    if count < 1 or column.size % count:
        count = 1
    return count


def solution(mesh):
    devices = np.asarray(mesh.devices)
    n_seg, n_mp, n_seq = devices.shape
    n_in = inner_size(mesh)
    split = Mesh(
        devices.reshape(n_seg, n_mp // n_in, n_in, n_seq), ("segment", OUTER, INNER, "seq")
    )
    placed = (
        P(MP, "segment", "seq", None, None),
        P(MP),
        P(MP),
        P(),
        P(None, "seq"),
        P("seq", "segment", None),
        P(MP, None, "seq", None, "segment", None),
    )
    out = P(MP, None, "seq", None, "segment", None)
    return jax.shard_map(
        on_device,
        mesh=split,
        in_specs=placed,
        out_specs=(out, out, out, out),
        check_vma=False,
    )
```

```python
import math

import jax
import jax.numpy as jnp
import numpy as np
from jax import lax
from jax.sharding import Mesh
from jax.sharding import PartitionSpec as P

OUTER = "mp_outer"
INNER = "mp_inner"
MP = (OUTER, INNER)
SLOT_MODE = 'bruck'
ROW_MODE = 'a2a'
FANOUT = 'a2a'
RAW = True


def passed_along(shard, axis, by):
    count = lax.axis_size(axis)
    pairs = [(i, i + by) for i in range(count) if 0 <= i + by < count]
    return lax.ppermute(shard, axis, pairs)


def swap_seq(x):
    return lax.ppermute(x, "seq", [(0, 1), (1, 0)])


def causal_conv(frames, conv_w):
    earlier = passed_along(frames[1:2], "segment", 1)[0]
    total = jnp.einsum("rcx,xy->rcy", frames[1], conv_w[0], preferred_element_type=jnp.float32)
    total = total + jnp.einsum(
        "rcx,xy->rcy", frames[0], conv_w[1], preferred_element_type=jnp.float32
    )
    total = total + jnp.einsum(
        "rcx,xy->rcy", earlier, conv_w[2], preferred_element_type=jnp.float32
    )
    return jax.nn.silu(total).astype(jnp.bfloat16)


def gather_rotated(x, axis):
    n = lax.axis_size(axis)
    have = x[None]
    shift = 1
    while have.shape[0] < n:
        need = min(have.shape[0], n - have.shape[0])
        pairs = [(j, (j - shift) % n) for j in range(n)]
        have = jnp.concatenate([have, lax.ppermute(have[:need], axis, pairs)], axis=0)
        shift *= 2
    return have


def gather_ordered(x, axis):
    n = lax.axis_size(axis)
    have = gather_rotated(x, axis)
    if n == 1:
        return have
    me = lax.axis_index(axis)
    return jnp.take(have, (jnp.arange(n) - me) % n, axis=0)


def gather_a2a(x, axis):
    n = lax.axis_size(axis)
    send = jnp.broadcast_to(x[None], (n,) + x.shape)
    return lax.all_to_all(send, axis, 0, 0, tiled=True)


def gather(x, axis, mode):
    if mode == "a2a":
        return gather_a2a(x, axis)
    if mode == "ag":
        return lax.all_gather(x, axis, axis=0)
    return gather_ordered(x, axis)


def route(piece, tokenizer_slot):
    n_in = lax.axis_size(INNER)
    n_out = lax.axis_size(OUTER)
    my_out = lax.axis_index(OUTER)
    source = tokenizer_slot[0]
    wanted = gather(tokenizer_slot, OUTER, SLOT_MODE)[:, 0]
    row = gather(piece, INNER, ROW_MODE)
    pick = jnp.clip(wanted % n_in, 0, n_in - 1)
    mine = (wanted // n_in) == my_out
    send = jnp.take(row, pick, axis=0)
    send = jnp.where(mine.reshape((n_out,) + (1,) * piece.ndim), send, jnp.zeros_like(send))
    origin = jnp.clip(source // n_in, 0, n_out - 1)
    if FANOUT == "merged":
        n_grp = lax.axis_size("segment") * lax.axis_size("seq")
        wide = jnp.broadcast_to(send[:, None], (n_out, n_grp) + piece.shape)
        wide = wide.reshape((n_out * n_grp,) + piece.shape)
        got = lax.all_to_all(wide, (OUTER, "segment", "seq"), 0, 0, tiled=True)
        got = got.reshape((n_out, n_grp) + piece.shape)
        return lax.dynamic_index_in_dim(got, origin, 0, keepdims=False)
    got = lax.all_to_all(send, OUTER, 0, 0, tiled=True)
    routed = lax.dynamic_index_in_dim(got, origin, 0, keepdims=False)
    return gather(routed, ("segment", "seq"), FANOUT)


def conv_all(frames, conv_w):
    current = frames[1::2]
    middle = frames[0::2]
    earlier = jnp.concatenate([jnp.zeros_like(current[:1]), current[:-1]], axis=0)
    total = jnp.einsum("frcx,xy->frcy", current, conv_w[0], preferred_element_type=jnp.float32)
    total = total + jnp.einsum(
        "frcx,xy->frcy", middle, conv_w[1], preferred_element_type=jnp.float32
    )
    total = total + jnp.einsum(
        "frcx,xy->frcy", earlier, conv_w[2], preferred_element_type=jnp.float32
    )
    return jax.nn.silu(total).astype(jnp.bfloat16)


def masked_scores(queries, keys, keep, scale):
    scores = jnp.einsum("qhd,khd->hqk", queries, keys, preferred_element_type=jnp.float32) * scale
    return jnp.where(keep[None, None, :], scores, -jnp.inf)


def on_device(frames_in, valid_frames, tokenizer_slot, conv_w, embed_w, qkv_w, out_grad):
    n_seg = lax.axis_size("segment")
    n_seq = lax.axis_size("seq")
    me = lax.axis_index("seq")
    if RAW:
        local = frames_in[0]
        n_fr, row_dev, cols, channels = local.shape
        pieces = route(local, tokenizer_slot).reshape(
            (n_seg, n_seq, n_fr, row_dev, cols, channels)
        )
        frames = pieces.transpose(0, 2, 1, 3, 4, 5).reshape(
            n_seg * n_fr, n_seq * row_dev, cols, channels
        )
        act_all = conv_all(frames, conv_w).reshape(n_seg, n_seq, row_dev, cols, channels)
    else:
        act = causal_conv(frames_in[0], conv_w)
        row_dev, cols, channels = act.shape
        act_all = route(act, tokenizer_slot).reshape(n_seg, n_seq, row_dev, cols, channels)
    own_rows = lax.dynamic_index_in_dim(act_all, me, 1, keepdims=False)
    other_rows = lax.dynamic_index_in_dim(act_all, 1 - me, 1, keepdims=False)
    latent = jnp.stack([own_rows, other_rows], axis=1)
    heads_local = qkv_w.shape[1]
    head_size = qkv_w.shape[2] // 3
    rows = n_seq * row_dev

    def project(piece):
        hidden = jnp.einsum(
            "frcx,xd->frcd", piece, embed_w, preferred_element_type=jnp.float32
        ).astype(jnp.bfloat16)
        return jnp.einsum("frcd,dhe->frche", hidden, qkv_w, preferred_element_type=jnp.float32)

    received = swap_seq(project(latent[:, 1]))
    own_partial = lax.optimization_barrier(project(latent[:, 0]))
    own_qkv = (own_partial + received).astype(jnp.bfloat16)
    own_pair = own_qkv[..., head_size:]
    other_pair = swap_seq(own_pair)
    all_pair = jnp.concatenate([own_pair, other_pair], axis=1)
    queries5 = own_qkv[..., :head_size]
    scale = 1.0 / math.sqrt(head_size)
    n_query = n_seg * row_dev * cols
    n_key = n_seg * rows * cols
    q_flat = queries5.reshape(n_query, heads_local, head_size)
    keys = all_pair[..., :head_size].reshape(n_key, heads_local, head_size)
    values = all_pair[..., head_size:].reshape(n_key, heads_local, head_size)
    limit = valid_frames[0]
    keep = jnp.arange(n_key, dtype=jnp.int32) // (rows * cols) < limit
    scores = masked_scores(q_flat, keys, keep, scale)
    top = jnp.max(scores, axis=-1, keepdims=True)
    lse = top + jnp.log(jnp.sum(jnp.exp(scores - top), axis=-1, keepdims=True))
    prob = jnp.exp(scores - lse)
    prob_b = prob.astype(jnp.bfloat16)
    attn = jnp.einsum("hqk,khd->qhd", prob_b, values, preferred_element_type=jnp.float32).astype(
        jnp.bfloat16
    )
    grad = out_grad.reshape(n_query, heads_local, head_size)
    dprob = jnp.einsum("qhd,khd->hqk", grad, values, preferred_element_type=jnp.float32)
    delta = jnp.sum(grad.astype(jnp.float32) * attn.astype(jnp.float32), axis=-1).T
    dscore = (prob * (dprob - delta[:, :, None])).astype(jnp.bfloat16)
    q_grad = (
        jnp.einsum("hqk,khd->qhd", dscore, keys, preferred_element_type=jnp.float32) * scale
    ).astype(jnp.bfloat16)
    key_part = (
        jnp.einsum("hqk,qhd->khd", dscore, q_flat, preferred_element_type=jnp.float32) * scale
    ).astype(jnp.bfloat16)
    value_part = jnp.einsum(
        "hqk,qhd->khd", prob_b, grad, preferred_element_type=jnp.float32
    ).astype(jnp.bfloat16)
    kv_part = jnp.stack([key_part, value_part]).reshape(
        2, n_seg, 2, row_dev, cols, heads_local, head_size
    )
    kv_sum = kv_part[:, :, 0].astype(jnp.float32) + swap_seq(kv_part[:, :, 1]).astype(jnp.float32)
    kv_sum = kv_sum.astype(jnp.bfloat16)
    k_grad = kv_sum[0]
    v_grad = kv_sum[1]
    shape6 = (1, n_seg, row_dev, cols, heads_local, head_size)
    return (
        attn.reshape(shape6),
        q_grad.reshape(shape6),
        k_grad.reshape(shape6),
        v_grad.reshape(shape6),
    )


def inner_size(mesh):
    column = np.asarray(mesh.devices)[0, :, 0]
    try:
        count = len({d.coords[1] for d in column})
    except AttributeError:
        count = 1
    if count < 1 or column.size % count:
        count = 1
    return count


def solution(mesh):
    devices = np.asarray(mesh.devices)
    n_seg, n_mp, n_seq = devices.shape
    n_in = inner_size(mesh)
    split = Mesh(
        devices.reshape(n_seg, n_mp // n_in, n_in, n_seq), ("segment", OUTER, INNER, "seq")
    )
    placed = (
        P(MP, "segment", "seq", None, None),
        P(MP),
        P(MP),
        P(),
        P(None, "seq"),
        P("seq", "segment", None),
        P(MP, None, "seq", None, "segment", None),
    )
    out = P(MP, None, "seq", None, "segment", None)
    return jax.shard_map(
        on_device,
        mesh=split,
        in_specs=placed,
        out_specs=(out, out, out, out),
        check_vma=False,
    )
```

```python
import math

import jax
import jax.numpy as jnp
import numpy as np
from jax import lax
from jax.sharding import Mesh
from jax.sharding import PartitionSpec as P

OUTER = "mp_outer"
INNER = "mp_inner"
MP = (OUTER, INNER)
SLOT_MODE = 'a2a'
ROW_MODE = 'bruck'
FANOUT = 'a2a'
RAW = True


def passed_along(shard, axis, by):
    count = lax.axis_size(axis)
    pairs = [(i, i + by) for i in range(count) if 0 <= i + by < count]
    return lax.ppermute(shard, axis, pairs)


def swap_seq(x):
    return lax.ppermute(x, "seq", [(0, 1), (1, 0)])


def causal_conv(frames, conv_w):
    earlier = passed_along(frames[1:2], "segment", 1)[0]
    total = jnp.einsum("rcx,xy->rcy", frames[1], conv_w[0], preferred_element_type=jnp.float32)
    total = total + jnp.einsum(
        "rcx,xy->rcy", frames[0], conv_w[1], preferred_element_type=jnp.float32
    )
    total = total + jnp.einsum(
        "rcx,xy->rcy", earlier, conv_w[2], preferred_element_type=jnp.float32
    )
    return jax.nn.silu(total).astype(jnp.bfloat16)


def gather_rotated(x, axis):
    n = lax.axis_size(axis)
    have = x[None]
    shift = 1
    while have.shape[0] < n:
        need = min(have.shape[0], n - have.shape[0])
        pairs = [(j, (j - shift) % n) for j in range(n)]
        have = jnp.concatenate([have, lax.ppermute(have[:need], axis, pairs)], axis=0)
        shift *= 2
    return have


def gather_ordered(x, axis):
    n = lax.axis_size(axis)
    have = gather_rotated(x, axis)
    if n == 1:
        return have
    me = lax.axis_index(axis)
    return jnp.take(have, (jnp.arange(n) - me) % n, axis=0)


def gather_a2a(x, axis):
    n = lax.axis_size(axis)
    send = jnp.broadcast_to(x[None], (n,) + x.shape)
    return lax.all_to_all(send, axis, 0, 0, tiled=True)


def gather(x, axis, mode):
    if mode == "a2a":
        return gather_a2a(x, axis)
    if mode == "ag":
        return lax.all_gather(x, axis, axis=0)
    return gather_ordered(x, axis)


def route(piece, tokenizer_slot):
    n_in = lax.axis_size(INNER)
    n_out = lax.axis_size(OUTER)
    my_out = lax.axis_index(OUTER)
    source = tokenizer_slot[0]
    wanted = gather(tokenizer_slot, OUTER, SLOT_MODE)[:, 0]
    row = gather(piece, INNER, ROW_MODE)
    pick = jnp.clip(wanted % n_in, 0, n_in - 1)
    mine = (wanted // n_in) == my_out
    send = jnp.take(row, pick, axis=0)
    send = jnp.where(mine.reshape((n_out,) + (1,) * piece.ndim), send, jnp.zeros_like(send))
    origin = jnp.clip(source // n_in, 0, n_out - 1)
    if FANOUT == "merged":
        n_grp = lax.axis_size("segment") * lax.axis_size("seq")
        wide = jnp.broadcast_to(send[:, None], (n_out, n_grp) + piece.shape)
        wide = wide.reshape((n_out * n_grp,) + piece.shape)
        got = lax.all_to_all(wide, (OUTER, "segment", "seq"), 0, 0, tiled=True)
        got = got.reshape((n_out, n_grp) + piece.shape)
        return lax.dynamic_index_in_dim(got, origin, 0, keepdims=False)
    got = lax.all_to_all(send, OUTER, 0, 0, tiled=True)
    routed = lax.dynamic_index_in_dim(got, origin, 0, keepdims=False)
    return gather(routed, ("segment", "seq"), FANOUT)


def conv_all(frames, conv_w):
    current = frames[1::2]
    middle = frames[0::2]
    earlier = jnp.concatenate([jnp.zeros_like(current[:1]), current[:-1]], axis=0)
    total = jnp.einsum("frcx,xy->frcy", current, conv_w[0], preferred_element_type=jnp.float32)
    total = total + jnp.einsum(
        "frcx,xy->frcy", middle, conv_w[1], preferred_element_type=jnp.float32
    )
    total = total + jnp.einsum(
        "frcx,xy->frcy", earlier, conv_w[2], preferred_element_type=jnp.float32
    )
    return jax.nn.silu(total).astype(jnp.bfloat16)


def masked_scores(queries, keys, keep, scale):
    scores = jnp.einsum("qhd,khd->hqk", queries, keys, preferred_element_type=jnp.float32) * scale
    return jnp.where(keep[None, None, :], scores, -jnp.inf)


def on_device(frames_in, valid_frames, tokenizer_slot, conv_w, embed_w, qkv_w, out_grad):
    n_seg = lax.axis_size("segment")
    n_seq = lax.axis_size("seq")
    me = lax.axis_index("seq")
    if RAW:
        local = frames_in[0]
        n_fr, row_dev, cols, channels = local.shape
        pieces = route(local, tokenizer_slot).reshape(
            (n_seg, n_seq, n_fr, row_dev, cols, channels)
        )
        frames = pieces.transpose(0, 2, 1, 3, 4, 5).reshape(
            n_seg * n_fr, n_seq * row_dev, cols, channels
        )
        act_all = conv_all(frames, conv_w).reshape(n_seg, n_seq, row_dev, cols, channels)
    else:
        act = causal_conv(frames_in[0], conv_w)
        row_dev, cols, channels = act.shape
        act_all = route(act, tokenizer_slot).reshape(n_seg, n_seq, row_dev, cols, channels)
    own_rows = lax.dynamic_index_in_dim(act_all, me, 1, keepdims=False)
    other_rows = lax.dynamic_index_in_dim(act_all, 1 - me, 1, keepdims=False)
    latent = jnp.stack([own_rows, other_rows], axis=1)
    heads_local = qkv_w.shape[1]
    head_size = qkv_w.shape[2] // 3
    rows = n_seq * row_dev

    def project(piece):
        hidden = jnp.einsum(
            "...x,xd->...d", piece, embed_w, preferred_element_type=jnp.float32
        ).astype(jnp.bfloat16)
        return jnp.einsum("...d,dhe->...he", hidden, qkv_w, preferred_element_type=jnp.float32)

    partial_qkv = project(latent)
    own_qkv = (partial_qkv[:, 0] + swap_seq(partial_qkv[:, 1])).astype(jnp.bfloat16)
    own_pair = own_qkv[..., head_size:]
    other_pair = swap_seq(own_pair)
    all_pair = jnp.concatenate([own_pair, other_pair], axis=1)
    queries5 = own_qkv[..., :head_size]
    scale = 1.0 / math.sqrt(head_size)
    n_query = n_seg * row_dev * cols
    n_key = n_seg * rows * cols
    q_flat = queries5.reshape(n_query, heads_local, head_size)
    keys = all_pair[..., :head_size].reshape(n_key, heads_local, head_size)
    values = all_pair[..., head_size:].reshape(n_key, heads_local, head_size)
    limit = valid_frames[0]
    keep = jnp.arange(n_key, dtype=jnp.int32) // (rows * cols) < limit
    scores = masked_scores(q_flat, keys, keep, scale)
    top = jnp.max(scores, axis=-1, keepdims=True)
    lse = top + jnp.log(jnp.sum(jnp.exp(scores - top), axis=-1, keepdims=True))
    prob = jnp.exp(scores - lse)
    prob_b = prob.astype(jnp.bfloat16)
    attn = jnp.einsum("hqk,khd->qhd", prob_b, values, preferred_element_type=jnp.float32).astype(
        jnp.bfloat16
    )
    grad = out_grad.reshape(n_query, heads_local, head_size)
    dprob = jnp.einsum("qhd,khd->hqk", grad, values, preferred_element_type=jnp.float32)
    delta = jnp.sum(grad.astype(jnp.float32) * attn.astype(jnp.float32), axis=-1).T
    dscore = (prob * (dprob - delta[:, :, None])).astype(jnp.bfloat16)
    q_grad = (
        jnp.einsum("hqk,khd->qhd", dscore, keys, preferred_element_type=jnp.float32) * scale
    ).astype(jnp.bfloat16)
    key_part = (
        jnp.einsum("hqk,qhd->khd", dscore, q_flat, preferred_element_type=jnp.float32) * scale
    ).astype(jnp.bfloat16)
    value_part = jnp.einsum(
        "hqk,qhd->khd", prob_b, grad, preferred_element_type=jnp.float32
    ).astype(jnp.bfloat16)
    kv_part = jnp.stack([key_part, value_part]).reshape(
        2, n_seg, 2, row_dev, cols, heads_local, head_size
    )
    kv_sum = kv_part[:, :, 0].astype(jnp.float32) + swap_seq(kv_part[:, :, 1]).astype(jnp.float32)
    kv_sum = kv_sum.astype(jnp.bfloat16)
    k_grad = kv_sum[0]
    v_grad = kv_sum[1]
    shape6 = (1, n_seg, row_dev, cols, heads_local, head_size)
    return (
        attn.reshape(shape6),
        q_grad.reshape(shape6),
        k_grad.reshape(shape6),
        v_grad.reshape(shape6),
    )


def inner_size(mesh):
    column = np.asarray(mesh.devices)[0, :, 0]
    try:
        count = len({d.coords[1] for d in column})
    except AttributeError:
        count = 1
    if count < 1 or column.size % count:
        count = 1
    return count


def solution(mesh):
    devices = np.asarray(mesh.devices)
    n_seg, n_mp, n_seq = devices.shape
    n_in = inner_size(mesh)
    split = Mesh(
        devices.reshape(n_seg, n_mp // n_in, n_in, n_seq), ("segment", OUTER, INNER, "seq")
    )
    placed = (
        P(MP, "segment", "seq", None, None),
        P(MP),
        P(MP),
        P(),
        P(None, "seq"),
        P("seq", "segment", None),
        P(MP, None, "seq", None, "segment", None),
    )
    out = P(MP, None, "seq", None, "segment", None)
    return jax.shard_map(
        on_device,
        mesh=split,
        in_specs=placed,
        out_specs=(out, out, out, out),
        check_vma=False,
    )
```

```python
import math

import jax
import jax.numpy as jnp
import numpy as np
from jax import lax
from jax.sharding import Mesh
from jax.sharding import PartitionSpec as P

OUTER = "mp_outer"
INNER = "mp_inner"
MP = (OUTER, INNER)
SLOT_MODE = 'a2a'
ROW_MODE = 'a2a'
FANOUT = 'a2a'
RAW = True


def passed_along(shard, axis, by):
    count = lax.axis_size(axis)
    pairs = [(i, i + by) for i in range(count) if 0 <= i + by < count]
    return lax.ppermute(shard, axis, pairs)


def swap_seq(x):
    return lax.ppermute(x, "seq", [(0, 1), (1, 0)])


def causal_conv(frames, conv_w):
    earlier = passed_along(frames[1:2], "segment", 1)[0]
    total = jnp.einsum("rcx,xy->rcy", frames[1], conv_w[0], preferred_element_type=jnp.float32)
    total = total + jnp.einsum(
        "rcx,xy->rcy", frames[0], conv_w[1], preferred_element_type=jnp.float32
    )
    total = total + jnp.einsum(
        "rcx,xy->rcy", earlier, conv_w[2], preferred_element_type=jnp.float32
    )
    return jax.nn.silu(total).astype(jnp.bfloat16)


def gather_rotated(x, axis):
    n = lax.axis_size(axis)
    have = x[None]
    shift = 1
    while have.shape[0] < n:
        need = min(have.shape[0], n - have.shape[0])
        pairs = [(j, (j - shift) % n) for j in range(n)]
        have = jnp.concatenate([have, lax.ppermute(have[:need], axis, pairs)], axis=0)
        shift *= 2
    return have


def gather_ordered(x, axis):
    n = lax.axis_size(axis)
    have = gather_rotated(x, axis)
    if n == 1:
        return have
    me = lax.axis_index(axis)
    return jnp.take(have, (jnp.arange(n) - me) % n, axis=0)


def gather_a2a(x, axis):
    n = lax.axis_size(axis)
    send = jnp.broadcast_to(x[None], (n,) + x.shape)
    return lax.all_to_all(send, axis, 0, 0, tiled=True)


def gather(x, axis, mode):
    if mode == "a2a":
        return gather_a2a(x, axis)
    if mode == "ag":
        return lax.all_gather(x, axis, axis=0)
    return gather_ordered(x, axis)


def route(piece, tokenizer_slot):
    n_in = lax.axis_size(INNER)
    n_out = lax.axis_size(OUTER)
    my_out = lax.axis_index(OUTER)
    source = tokenizer_slot[0]
    wanted = gather(tokenizer_slot, OUTER, SLOT_MODE)[:, 0]
    row = gather(piece, INNER, ROW_MODE)
    pick = jnp.clip(wanted % n_in, 0, n_in - 1)
    mine = (wanted // n_in) == my_out
    send = jnp.take(row, pick, axis=0)
    send = jnp.where(mine.reshape((n_out,) + (1,) * piece.ndim), send, jnp.zeros_like(send))
    origin = jnp.clip(source // n_in, 0, n_out - 1)
    if FANOUT == "merged":
        n_grp = lax.axis_size("segment") * lax.axis_size("seq")
        wide = jnp.broadcast_to(send[:, None], (n_out, n_grp) + piece.shape)
        wide = wide.reshape((n_out * n_grp,) + piece.shape)
        got = lax.all_to_all(wide, (OUTER, "segment", "seq"), 0, 0, tiled=True)
        got = got.reshape((n_out, n_grp) + piece.shape)
        return lax.dynamic_index_in_dim(got, origin, 0, keepdims=False)
    got = lax.all_to_all(send, OUTER, 0, 0, tiled=True)
    routed = lax.dynamic_index_in_dim(got, origin, 0, keepdims=False)
    return gather(routed, ("segment", "seq"), FANOUT)


def conv_all(frames, conv_w):
    current = frames[1::2]
    middle = frames[0::2]
    earlier = jnp.concatenate([jnp.zeros_like(current[:1]), current[:-1]], axis=0)
    total = jnp.einsum("frcx,xy->frcy", current, conv_w[0], preferred_element_type=jnp.float32)
    total = total + jnp.einsum(
        "frcx,xy->frcy", middle, conv_w[1], preferred_element_type=jnp.float32
    )
    total = total + jnp.einsum(
        "frcx,xy->frcy", earlier, conv_w[2], preferred_element_type=jnp.float32
    )
    return jax.nn.silu(total).astype(jnp.bfloat16)


def masked_scores(queries, keys, keep, scale):
    scores = jnp.einsum("qhd,khd->hqk", queries, keys, preferred_element_type=jnp.float32) * scale
    return jnp.where(keep[None, None, :], scores, -jnp.inf)


def on_device(frames_in, valid_frames, tokenizer_slot, conv_w, embed_w, qkv_w, out_grad):
    n_seg = lax.axis_size("segment")
    n_seq = lax.axis_size("seq")
    me = lax.axis_index("seq")
    if RAW:
        local = frames_in[0]
        n_fr, row_dev, cols, channels = local.shape
        pieces = route(local, tokenizer_slot).reshape(
            (n_seg, n_seq, n_fr, row_dev, cols, channels)
        )
        frames = pieces.transpose(0, 2, 1, 3, 4, 5).reshape(
            n_seg * n_fr, n_seq * row_dev, cols, channels
        )
        act_all = conv_all(frames, conv_w).reshape(n_seg, n_seq, row_dev, cols, channels)
    else:
        act = causal_conv(frames_in[0], conv_w)
        row_dev, cols, channels = act.shape
        act_all = route(act, tokenizer_slot).reshape(n_seg, n_seq, row_dev, cols, channels)
    own_rows = lax.dynamic_index_in_dim(act_all, me, 1, keepdims=False)
    other_rows = lax.dynamic_index_in_dim(act_all, 1 - me, 1, keepdims=False)
    latent = jnp.stack([own_rows, other_rows], axis=1)
    heads_local = qkv_w.shape[1]
    head_size = qkv_w.shape[2] // 3
    rows = n_seq * row_dev

    def project(piece):
        hidden = jnp.einsum(
            "...x,xd->...d", piece, embed_w, preferred_element_type=jnp.float32
        ).astype(jnp.bfloat16)
        return jnp.einsum("...d,dhe->...he", hidden, qkv_w, preferred_element_type=jnp.float32)

    partial_qkv = project(latent)
    own_qkv = (partial_qkv[:, 0] + swap_seq(partial_qkv[:, 1])).astype(jnp.bfloat16)
    own_pair = own_qkv[..., head_size:]
    other_pair = swap_seq(own_pair)
    all_pair = jnp.concatenate([own_pair, other_pair], axis=1)
    queries5 = own_qkv[..., :head_size]
    scale = 1.0 / math.sqrt(head_size)
    n_query = n_seg * row_dev * cols
    n_key = n_seg * rows * cols
    q_flat = queries5.reshape(n_query, heads_local, head_size)
    keys = all_pair[..., :head_size].reshape(n_key, heads_local, head_size)
    values = all_pair[..., head_size:].reshape(n_key, heads_local, head_size)
    limit = valid_frames[0]
    keep = jnp.arange(n_key, dtype=jnp.int32) // (rows * cols) < limit
    scores = masked_scores(q_flat, keys, keep, scale)
    top = jnp.max(scores, axis=-1, keepdims=True)
    lse = top + jnp.log(jnp.sum(jnp.exp(scores - top), axis=-1, keepdims=True))
    prob = jnp.exp(scores - lse)
    prob_b = prob.astype(jnp.bfloat16)
    attn = jnp.einsum("hqk,khd->qhd", prob_b, values, preferred_element_type=jnp.float32).astype(
        jnp.bfloat16
    )
    grad = out_grad.reshape(n_query, heads_local, head_size)
    dprob = jnp.einsum("qhd,khd->hqk", grad, values, preferred_element_type=jnp.float32)
    delta = jnp.sum(grad.astype(jnp.float32) * attn.astype(jnp.float32), axis=-1).T
    dscore = (prob * (dprob - delta[:, :, None])).astype(jnp.bfloat16)
    q_grad = (
        jnp.einsum("hqk,khd->qhd", dscore, keys, preferred_element_type=jnp.float32) * scale
    ).astype(jnp.bfloat16)
    key_part = (
        jnp.einsum("hqk,qhd->khd", dscore, q_flat, preferred_element_type=jnp.float32) * scale
    ).astype(jnp.bfloat16)
    value_part = jnp.einsum(
        "hqk,qhd->khd", prob_b, grad, preferred_element_type=jnp.float32
    ).astype(jnp.bfloat16)
    kv_part = jnp.stack([key_part, value_part]).reshape(
        2, n_seg, 2, row_dev, cols, heads_local, head_size
    )
    kv_sum = kv_part[:, :, 0].astype(jnp.float32) + swap_seq(kv_part[:, :, 1]).astype(jnp.float32)
    kv_sum = kv_sum.astype(jnp.bfloat16)
    k_grad = kv_sum[0]
    v_grad = kv_sum[1]
    shape6 = (1, n_seg, row_dev, cols, heads_local, head_size)
    return (
        attn.reshape(shape6),
        q_grad.reshape(shape6),
        k_grad.reshape(shape6),
        v_grad.reshape(shape6),
    )


def inner_size(mesh):
    column = np.asarray(mesh.devices)[0, :, 0]
    try:
        count = len({d.coords[1] for d in column})
    except AttributeError:
        count = 1
    if count < 1 or column.size % count:
        count = 1
    return count


def solution(mesh):
    devices = np.asarray(mesh.devices)
    n_seg, n_mp, n_seq = devices.shape
    n_in = inner_size(mesh)
    split = Mesh(
        devices.reshape(n_seg, n_mp // n_in, n_in, n_seq), ("segment", OUTER, INNER, "seq")
    )
    placed = (
        P(MP, "segment", "seq", None, None),
        P(MP),
        P(MP),
        P(),
        P(None, "seq"),
        P("seq", "segment", None),
        P(MP, None, "seq", None, "segment", None),
    )
    out = P(MP, None, "seq", None, "segment", None)
    return jax.shard_map(
        on_device,
        mesh=split,
        in_specs=placed,
        out_specs=(out, out, out, out),
        check_vma=False,
    )
```

```python
import math

import jax
import jax.numpy as jnp
import numpy as np
from jax import lax
from jax.sharding import Mesh
from jax.sharding import PartitionSpec as P

OUTER = "mp_outer"
INNER = "mp_inner"
MP = (OUTER, INNER)
SLOT_MODE = 'a2a'
ROW_MODE = 'a2a'
FANOUT = 'a2a'
RAW = False


def passed_along(shard, axis, by):
    count = lax.axis_size(axis)
    pairs = [(i, i + by) for i in range(count) if 0 <= i + by < count]
    return lax.ppermute(shard, axis, pairs)


def swap_seq(x):
    return lax.ppermute(x, "seq", [(0, 1), (1, 0)])


def causal_conv(frames, conv_w):
    earlier = passed_along(frames[1:2], "segment", 1)[0]
    total = jnp.einsum("rcx,xy->rcy", frames[1], conv_w[0], preferred_element_type=jnp.float32)
    total = total + jnp.einsum(
        "rcx,xy->rcy", frames[0], conv_w[1], preferred_element_type=jnp.float32
    )
    total = total + jnp.einsum(
        "rcx,xy->rcy", earlier, conv_w[2], preferred_element_type=jnp.float32
    )
    return jax.nn.silu(total).astype(jnp.bfloat16)


def gather_rotated(x, axis):
    n = lax.axis_size(axis)
    have = x[None]
    shift = 1
    while have.shape[0] < n:
        need = min(have.shape[0], n - have.shape[0])
        pairs = [(j, (j - shift) % n) for j in range(n)]
        have = jnp.concatenate([have, lax.ppermute(have[:need], axis, pairs)], axis=0)
        shift *= 2
    return have


def gather_ordered(x, axis):
    n = lax.axis_size(axis)
    have = gather_rotated(x, axis)
    if n == 1:
        return have
    me = lax.axis_index(axis)
    return jnp.take(have, (jnp.arange(n) - me) % n, axis=0)


def gather_a2a(x, axis):
    n = lax.axis_size(axis)
    send = jnp.broadcast_to(x[None], (n,) + x.shape)
    return lax.all_to_all(send, axis, 0, 0, tiled=True)


def gather(x, axis, mode):
    if mode == "a2a":
        return gather_a2a(x, axis)
    if mode == "ag":
        return lax.all_gather(x, axis, axis=0)
    return gather_ordered(x, axis)


def route(piece, tokenizer_slot):
    n_in = lax.axis_size(INNER)
    n_out = lax.axis_size(OUTER)
    my_out = lax.axis_index(OUTER)
    source = tokenizer_slot[0]
    wanted = gather(tokenizer_slot, OUTER, SLOT_MODE)[:, 0]
    row = gather(piece, INNER, ROW_MODE)
    pick = jnp.clip(wanted % n_in, 0, n_in - 1)
    mine = (wanted // n_in) == my_out
    send = jnp.take(row, pick, axis=0)
    send = jnp.where(mine.reshape((n_out,) + (1,) * piece.ndim), send, jnp.zeros_like(send))
    origin = jnp.clip(source // n_in, 0, n_out - 1)
    if FANOUT == "merged":
        n_grp = lax.axis_size("segment") * lax.axis_size("seq")
        wide = jnp.broadcast_to(send[:, None], (n_out, n_grp) + piece.shape)
        wide = wide.reshape((n_out * n_grp,) + piece.shape)
        got = lax.all_to_all(wide, (OUTER, "segment", "seq"), 0, 0, tiled=True)
        got = got.reshape((n_out, n_grp) + piece.shape)
        return lax.dynamic_index_in_dim(got, origin, 0, keepdims=False)
    got = lax.all_to_all(send, OUTER, 0, 0, tiled=True)
    routed = lax.dynamic_index_in_dim(got, origin, 0, keepdims=False)
    return gather(routed, ("segment", "seq"), FANOUT)


def conv_all(frames, conv_w):
    current = frames[1::2]
    middle = frames[0::2]
    earlier = jnp.concatenate([jnp.zeros_like(current[:1]), current[:-1]], axis=0)
    total = jnp.einsum("frcx,xy->frcy", current, conv_w[0], preferred_element_type=jnp.float32)
    total = total + jnp.einsum(
        "frcx,xy->frcy", middle, conv_w[1], preferred_element_type=jnp.float32
    )
    total = total + jnp.einsum(
        "frcx,xy->frcy", earlier, conv_w[2], preferred_element_type=jnp.float32
    )
    return jax.nn.silu(total).astype(jnp.bfloat16)


def masked_scores(queries, keys, keep, scale):
    scores = jnp.einsum("qhd,khd->hqk", queries, keys, preferred_element_type=jnp.float32) * scale
    return jnp.where(keep[None, None, :], scores, -jnp.inf)


def on_device(frames_in, valid_frames, tokenizer_slot, conv_w, embed_w, qkv_w, out_grad):
    n_seg = lax.axis_size("segment")
    n_seq = lax.axis_size("seq")
    me = lax.axis_index("seq")
    if RAW:
        local = frames_in[0]
        n_fr, row_dev, cols, channels = local.shape
        pieces = route(local, tokenizer_slot).reshape(
            (n_seg, n_seq, n_fr, row_dev, cols, channels)
        )
        frames = pieces.transpose(0, 2, 1, 3, 4, 5).reshape(
            n_seg * n_fr, n_seq * row_dev, cols, channels
        )
        act_all = conv_all(frames, conv_w).reshape(n_seg, n_seq, row_dev, cols, channels)
    else:
        act = causal_conv(frames_in[0], conv_w)
        row_dev, cols, channels = act.shape
        act_all = route(act, tokenizer_slot).reshape(n_seg, n_seq, row_dev, cols, channels)
    own_rows = lax.dynamic_index_in_dim(act_all, me, 1, keepdims=False)
    other_rows = lax.dynamic_index_in_dim(act_all, 1 - me, 1, keepdims=False)
    latent = jnp.stack([own_rows, other_rows], axis=1)
    heads_local = qkv_w.shape[1]
    head_size = qkv_w.shape[2] // 3
    rows = n_seq * row_dev

    def project(piece):
        hidden = jnp.einsum(
            "...x,xd->...d", piece, embed_w, preferred_element_type=jnp.float32
        ).astype(jnp.bfloat16)
        return jnp.einsum("...d,dhe->...he", hidden, qkv_w, preferred_element_type=jnp.float32)

    partial_qkv = project(latent)
    own_qkv = (partial_qkv[:, 0] + swap_seq(partial_qkv[:, 1])).astype(jnp.bfloat16)
    own_pair = own_qkv[..., head_size:]
    other_pair = swap_seq(own_pair)
    all_pair = jnp.concatenate([own_pair, other_pair], axis=1)
    queries5 = own_qkv[..., :head_size]
    scale = 1.0 / math.sqrt(head_size)
    n_query = n_seg * row_dev * cols
    n_key = n_seg * rows * cols
    q_flat = queries5.reshape(n_query, heads_local, head_size)
    keys = all_pair[..., :head_size].reshape(n_key, heads_local, head_size)
    values = all_pair[..., head_size:].reshape(n_key, heads_local, head_size)
    limit = valid_frames[0]
    keep = jnp.arange(n_key, dtype=jnp.int32) // (rows * cols) < limit
    scores = masked_scores(q_flat, keys, keep, scale)
    top = jnp.max(scores, axis=-1, keepdims=True)
    lse = top + jnp.log(jnp.sum(jnp.exp(scores - top), axis=-1, keepdims=True))
    prob = jnp.exp(scores - lse)
    prob_b = prob.astype(jnp.bfloat16)
    attn = jnp.einsum("hqk,khd->qhd", prob_b, values, preferred_element_type=jnp.float32).astype(
        jnp.bfloat16
    )
    grad = out_grad.reshape(n_query, heads_local, head_size)
    dprob = jnp.einsum("qhd,khd->hqk", grad, values, preferred_element_type=jnp.float32)
    delta = jnp.sum(grad.astype(jnp.float32) * attn.astype(jnp.float32), axis=-1).T
    dscore = (prob * (dprob - delta[:, :, None])).astype(jnp.bfloat16)
    q_grad = (
        jnp.einsum("hqk,khd->qhd", dscore, keys, preferred_element_type=jnp.float32) * scale
    ).astype(jnp.bfloat16)
    key_part = (
        jnp.einsum("hqk,qhd->khd", dscore, q_flat, preferred_element_type=jnp.float32) * scale
    ).astype(jnp.bfloat16)
    value_part = jnp.einsum(
        "hqk,qhd->khd", prob_b, grad, preferred_element_type=jnp.float32
    ).astype(jnp.bfloat16)
    kv_part = jnp.stack([key_part, value_part]).reshape(
        2, n_seg, 2, row_dev, cols, heads_local, head_size
    )
    kv_sum = kv_part[:, :, 0].astype(jnp.float32) + swap_seq(kv_part[:, :, 1]).astype(jnp.float32)
    kv_sum = kv_sum.astype(jnp.bfloat16)
    k_grad = kv_sum[0]
    v_grad = kv_sum[1]
    shape6 = (1, n_seg, row_dev, cols, heads_local, head_size)
    return (
        attn.reshape(shape6),
        q_grad.reshape(shape6),
        k_grad.reshape(shape6),
        v_grad.reshape(shape6),
    )


def inner_size(mesh):
    column = np.asarray(mesh.devices)[0, :, 0]
    try:
        count = len({d.coords[1] for d in column})
    except AttributeError:
        count = 1
    if count < 1 or column.size % count:
        count = 1
    return count


def solution(mesh):
    devices = np.asarray(mesh.devices)
    n_seg, n_mp, n_seq = devices.shape
    n_in = inner_size(mesh)
    split = Mesh(
        devices.reshape(n_seg, n_mp // n_in, n_in, n_seq), ("segment", OUTER, INNER, "seq")
    )
    placed = (
        P(MP, "segment", "seq", None, None),
        P(MP),
        P(MP),
        P(),
        P(None, "seq"),
        P("seq", "segment", None),
        P(MP, None, "seq", None, "segment", None),
    )
    out = P(MP, None, "seq", None, "segment", None)
    return jax.shard_map(
        on_device,
        mesh=split,
        in_specs=placed,
        out_specs=(out, out, out, out),
        check_vma=False,
    )
```

```python
import math

import jax
import jax.numpy as jnp
import numpy as np
from jax import lax
from jax.sharding import Mesh
from jax.sharding import PartitionSpec as P

OUTER = "mp_outer"
INNER = "mp_inner"
MP = (OUTER, INNER)
SLOT_MODE = 'a2a'
ROW_MODE = 'a2a'
FANOUT = 'a2a'
RAW = False


def passed_along(shard, axis, by):
    count = lax.axis_size(axis)
    pairs = [(i, i + by) for i in range(count) if 0 <= i + by < count]
    return lax.ppermute(shard, axis, pairs)


def swap_seq(x):
    return lax.ppermute(x, "seq", [(0, 1), (1, 0)])


def causal_conv(frames, conv_w):
    earlier = passed_along(frames[1:2], "segment", 1)[0]
    total = jnp.einsum("rcx,xy->rcy", frames[1], conv_w[0], preferred_element_type=jnp.float32)
    total = total + jnp.einsum(
        "rcx,xy->rcy", frames[0], conv_w[1], preferred_element_type=jnp.float32
    )
    total = total + jnp.einsum(
        "rcx,xy->rcy", earlier, conv_w[2], preferred_element_type=jnp.float32
    )
    return jax.nn.silu(total).astype(jnp.bfloat16)


def gather_rotated(x, axis):
    n = lax.axis_size(axis)
    have = x[None]
    shift = 1
    while have.shape[0] < n:
        need = min(have.shape[0], n - have.shape[0])
        pairs = [(j, (j - shift) % n) for j in range(n)]
        have = jnp.concatenate([have, lax.ppermute(have[:need], axis, pairs)], axis=0)
        shift *= 2
    return have


def gather_ordered(x, axis):
    n = lax.axis_size(axis)
    have = gather_rotated(x, axis)
    if n == 1:
        return have
    me = lax.axis_index(axis)
    return jnp.take(have, (jnp.arange(n) - me) % n, axis=0)


def gather_a2a(x, axis):
    n = lax.axis_size(axis)
    send = jnp.broadcast_to(x[None], (n,) + x.shape)
    return lax.all_to_all(send, axis, 0, 0, tiled=True)


def gather(x, axis, mode):
    if mode == "a2a":
        return gather_a2a(x, axis)
    if mode == "ag":
        return lax.all_gather(x, axis, axis=0)
    return gather_ordered(x, axis)


def route(piece, tokenizer_slot):
    n_in = lax.axis_size(INNER)
    n_out = lax.axis_size(OUTER)
    my_out = lax.axis_index(OUTER)
    source = tokenizer_slot[0]
    my_in = lax.axis_index(INNER)
    wanted = gather(tokenizer_slot, INNER, SLOT_MODE)[:, 0]
    column = gather(piece, OUTER, ROW_MODE)
    pick = jnp.clip(wanted // n_in, 0, n_out - 1)
    mine = (wanted % n_in) == my_in
    send = jnp.take(column, pick, axis=0)
    send = jnp.where(mine.reshape((n_in,) + (1,) * piece.ndim), send, jnp.zeros_like(send))
    origin = jnp.clip(source % n_in, 0, n_in - 1)
    got = lax.all_to_all(send, INNER, 0, 0, tiled=True)
    routed = lax.dynamic_index_in_dim(got, origin, 0, keepdims=False)
    return gather(routed, ("segment", "seq"), FANOUT)


def conv_all(frames, conv_w):
    current = frames[1::2]
    middle = frames[0::2]
    earlier = jnp.concatenate([jnp.zeros_like(current[:1]), current[:-1]], axis=0)
    total = jnp.einsum("frcx,xy->frcy", current, conv_w[0], preferred_element_type=jnp.float32)
    total = total + jnp.einsum(
        "frcx,xy->frcy", middle, conv_w[1], preferred_element_type=jnp.float32
    )
    total = total + jnp.einsum(
        "frcx,xy->frcy", earlier, conv_w[2], preferred_element_type=jnp.float32
    )
    return jax.nn.silu(total).astype(jnp.bfloat16)


def masked_scores(queries, keys, keep, scale):
    scores = jnp.einsum("qhd,khd->hqk", queries, keys, preferred_element_type=jnp.float32) * scale
    return jnp.where(keep[None, None, :], scores, -jnp.inf)


def on_device(frames_in, valid_frames, tokenizer_slot, conv_w, embed_w, qkv_w, out_grad):
    n_seg = lax.axis_size("segment")
    n_seq = lax.axis_size("seq")
    me = lax.axis_index("seq")
    if RAW:
        local = frames_in[0]
        n_fr, row_dev, cols, channels = local.shape
        pieces = route(local, tokenizer_slot).reshape(
            (n_seg, n_seq, n_fr, row_dev, cols, channels)
        )
        frames = pieces.transpose(0, 2, 1, 3, 4, 5).reshape(
            n_seg * n_fr, n_seq * row_dev, cols, channels
        )
        act_all = conv_all(frames, conv_w).reshape(n_seg, n_seq, row_dev, cols, channels)
    else:
        act = causal_conv(frames_in[0], conv_w)
        row_dev, cols, channels = act.shape
        act_all = route(act, tokenizer_slot).reshape(n_seg, n_seq, row_dev, cols, channels)
    own_rows = lax.dynamic_index_in_dim(act_all, me, 1, keepdims=False)
    other_rows = lax.dynamic_index_in_dim(act_all, 1 - me, 1, keepdims=False)
    latent = jnp.stack([own_rows, other_rows], axis=1)
    heads_local = qkv_w.shape[1]
    head_size = qkv_w.shape[2] // 3
    rows = n_seq * row_dev

    def project(piece):
        hidden = jnp.einsum(
            "...x,xd->...d", piece, embed_w, preferred_element_type=jnp.float32
        ).astype(jnp.bfloat16)
        return jnp.einsum("...d,dhe->...he", hidden, qkv_w, preferred_element_type=jnp.float32)

    partial_qkv = project(latent)
    own_qkv = (partial_qkv[:, 0] + swap_seq(partial_qkv[:, 1])).astype(jnp.bfloat16)
    own_pair = own_qkv[..., head_size:]
    other_pair = swap_seq(own_pair)
    all_pair = jnp.concatenate([own_pair, other_pair], axis=1)
    queries5 = own_qkv[..., :head_size]
    scale = 1.0 / math.sqrt(head_size)
    n_query = n_seg * row_dev * cols
    n_key = n_seg * rows * cols
    q_flat = queries5.reshape(n_query, heads_local, head_size)
    keys = all_pair[..., :head_size].reshape(n_key, heads_local, head_size)
    values = all_pair[..., head_size:].reshape(n_key, heads_local, head_size)
    limit = valid_frames[0]
    keep = jnp.arange(n_key, dtype=jnp.int32) // (rows * cols) < limit
    scores = masked_scores(q_flat, keys, keep, scale)
    top = jnp.max(scores, axis=-1, keepdims=True)
    lse = top + jnp.log(jnp.sum(jnp.exp(scores - top), axis=-1, keepdims=True))
    prob = jnp.exp(scores - lse)
    prob_b = prob.astype(jnp.bfloat16)
    attn = jnp.einsum("hqk,khd->qhd", prob_b, values, preferred_element_type=jnp.float32).astype(
        jnp.bfloat16
    )
    grad = out_grad.reshape(n_query, heads_local, head_size)
    dprob = jnp.einsum("qhd,khd->hqk", grad, values, preferred_element_type=jnp.float32)
    delta = jnp.sum(grad.astype(jnp.float32) * attn.astype(jnp.float32), axis=-1).T
    dscore = (prob * (dprob - delta[:, :, None])).astype(jnp.bfloat16)
    q_grad = (
        jnp.einsum("hqk,khd->qhd", dscore, keys, preferred_element_type=jnp.float32) * scale
    ).astype(jnp.bfloat16)
    key_part = (
        jnp.einsum("hqk,qhd->khd", dscore, q_flat, preferred_element_type=jnp.float32) * scale
    ).astype(jnp.bfloat16)
    value_part = jnp.einsum(
        "hqk,qhd->khd", prob_b, grad, preferred_element_type=jnp.float32
    ).astype(jnp.bfloat16)
    kv_part = jnp.stack([key_part, value_part]).reshape(
        2, n_seg, 2, row_dev, cols, heads_local, head_size
    )
    kv_sum = kv_part[:, :, 0].astype(jnp.float32) + swap_seq(kv_part[:, :, 1]).astype(jnp.float32)
    kv_sum = kv_sum.astype(jnp.bfloat16)
    k_grad = kv_sum[0]
    v_grad = kv_sum[1]
    shape6 = (1, n_seg, row_dev, cols, heads_local, head_size)
    return (
        attn.reshape(shape6),
        q_grad.reshape(shape6),
        k_grad.reshape(shape6),
        v_grad.reshape(shape6),
    )


def inner_size(mesh):
    column = np.asarray(mesh.devices)[0, :, 0]
    try:
        count = len({d.coords[1] for d in column})
    except AttributeError:
        count = 1
    if count < 1 or column.size % count:
        count = 1
    return count


def solution(mesh):
    devices = np.asarray(mesh.devices)
    n_seg, n_mp, n_seq = devices.shape
    n_in = inner_size(mesh)
    split = Mesh(
        devices.reshape(n_seg, n_mp // n_in, n_in, n_seq), ("segment", OUTER, INNER, "seq")
    )
    placed = (
        P(MP, "segment", "seq", None, None),
        P(MP),
        P(MP),
        P(),
        P(None, "seq"),
        P("seq", "segment", None),
        P(MP, None, "seq", None, "segment", None),
    )
    out = P(MP, None, "seq", None, "segment", None)
    return jax.shard_map(
        on_device,
        mesh=split,
        in_specs=placed,
        out_specs=(out, out, out, out),
        check_vma=False,
    )
```

```python
import math

import jax
import jax.numpy as jnp
import numpy as np
from jax import lax
from jax.sharding import Mesh
from jax.sharding import PartitionSpec as P

OUTER = "mp_outer"
INNER = "mp_inner"
MP = (OUTER, INNER)
SLOT_MODE = 'a2a'
ROW_MODE = 'a2a'
FANOUT = 'a2a'
RAW = False


def passed_along(shard, axis, by):
    count = lax.axis_size(axis)
    pairs = [(i, i + by) for i in range(count) if 0 <= i + by < count]
    return lax.ppermute(shard, axis, pairs)


def swap_seq(x):
    return lax.ppermute(x, "seq", [(0, 1), (1, 0)])


def causal_conv(frames, conv_w):
    earlier = passed_along(frames[1:2], "segment", 1)[0]
    total = jnp.einsum("rcx,xy->rcy", frames[1], conv_w[0], preferred_element_type=jnp.float32)
    total = total + jnp.einsum(
        "rcx,xy->rcy", frames[0], conv_w[1], preferred_element_type=jnp.float32
    )
    total = total + jnp.einsum(
        "rcx,xy->rcy", earlier, conv_w[2], preferred_element_type=jnp.float32
    )
    return jax.nn.silu(total).astype(jnp.bfloat16)


def gather_rotated(x, axis):
    n = lax.axis_size(axis)
    have = x[None]
    shift = 1
    while have.shape[0] < n:
        need = min(have.shape[0], n - have.shape[0])
        pairs = [(j, (j - shift) % n) for j in range(n)]
        have = jnp.concatenate([have, lax.ppermute(have[:need], axis, pairs)], axis=0)
        shift *= 2
    return have


def gather_ordered(x, axis):
    n = lax.axis_size(axis)
    have = gather_rotated(x, axis)
    if n == 1:
        return have
    me = lax.axis_index(axis)
    return jnp.take(have, (jnp.arange(n) - me) % n, axis=0)


def gather_a2a(x, axis):
    n = lax.axis_size(axis)
    send = jnp.broadcast_to(x[None], (n,) + x.shape)
    return lax.all_to_all(send, axis, 0, 0, tiled=True)


def gather(x, axis, mode):
    if mode == "a2a":
        return gather_a2a(x, axis)
    if mode == "ag":
        return lax.all_gather(x, axis, axis=0)
    return gather_ordered(x, axis)


def route(piece, tokenizer_slot):
    n_in = lax.axis_size(INNER)
    n_out = lax.axis_size(OUTER)
    my_out = lax.axis_index(OUTER)
    source = tokenizer_slot[0]
    my_in = lax.axis_index(INNER)
    wanted = gather(tokenizer_slot, INNER, SLOT_MODE)[:, 0]
    column = gather(piece, OUTER, ROW_MODE)
    pick = jnp.clip(wanted // n_in, 0, n_out - 1)
    mine = (wanted % n_in) == my_in
    send = jnp.take(column, pick, axis=0)
    send = jnp.where(mine.reshape((n_in,) + (1,) * piece.ndim), send, jnp.zeros_like(send))
    origin = jnp.clip(source % n_in, 0, n_in - 1)
    got = lax.all_to_all(send, INNER, 0, 0, tiled=True)
    routed = lax.dynamic_index_in_dim(got, origin, 0, keepdims=False)
    return gather(routed, ("segment", "seq"), FANOUT)


def conv_all(frames, conv_w):
    current = frames[1::2]
    middle = frames[0::2]
    earlier = jnp.concatenate([jnp.zeros_like(current[:1]), current[:-1]], axis=0)
    total = jnp.einsum("frcx,xy->frcy", current, conv_w[0], preferred_element_type=jnp.float32)
    total = total + jnp.einsum(
        "frcx,xy->frcy", middle, conv_w[1], preferred_element_type=jnp.float32
    )
    total = total + jnp.einsum(
        "frcx,xy->frcy", earlier, conv_w[2], preferred_element_type=jnp.float32
    )
    return jax.nn.silu(total).astype(jnp.bfloat16)


def masked_scores(queries, keys, keep, scale):
    scores = jnp.einsum("qhd,khd->hqk", queries, keys, preferred_element_type=jnp.float32) * scale
    return jnp.where(keep[None, None, :], scores, -jnp.inf)


def on_device(frames_in, valid_frames, tokenizer_slot, conv_w, embed_w, qkv_w, out_grad):
    n_seg = lax.axis_size("segment")
    n_seq = lax.axis_size("seq")
    me = lax.axis_index("seq")
    if RAW:
        local = frames_in[0]
        n_fr, row_dev, cols, channels = local.shape
        pieces = route(local, tokenizer_slot).reshape(
            (n_seg, n_seq, n_fr, row_dev, cols, channels)
        )
        frames = pieces.transpose(0, 2, 1, 3, 4, 5).reshape(
            n_seg * n_fr, n_seq * row_dev, cols, channels
        )
        act_all = conv_all(frames, conv_w).reshape(n_seg, n_seq, row_dev, cols, channels)
    else:
        act = causal_conv(frames_in[0], conv_w)
        row_dev, cols, channels = act.shape
        act_all = route(act, tokenizer_slot).reshape(n_seg, n_seq, row_dev, cols, channels)
    own_rows = lax.dynamic_index_in_dim(act_all, me, 1, keepdims=False)
    other_rows = lax.dynamic_index_in_dim(act_all, 1 - me, 1, keepdims=False)
    latent = jnp.stack([own_rows, other_rows], axis=1)
    heads_local = qkv_w.shape[1]
    head_size = qkv_w.shape[2] // 3
    rows = n_seq * row_dev

    def project(piece):
        hidden = jnp.einsum(
            "...x,xd->...d", piece, embed_w, preferred_element_type=jnp.float32
        ).astype(jnp.bfloat16)
        return jnp.einsum("...d,dhe->...he", hidden, qkv_w, preferred_element_type=jnp.float32)

    partial_qkv = project(latent)
    got_rows, got_pair = swap_seq((partial_qkv[:, 1], partial_qkv[:, 0, ..., head_size:]))
    own_qkv = (partial_qkv[:, 0] + got_rows).astype(jnp.bfloat16)
    own_pair = own_qkv[..., head_size:]
    other_pair = (partial_qkv[:, 1, ..., head_size:] + got_pair).astype(jnp.bfloat16)
    all_pair = jnp.concatenate([own_pair, other_pair], axis=1)
    queries5 = own_qkv[..., :head_size]
    scale = 1.0 / math.sqrt(head_size)
    n_query = n_seg * row_dev * cols
    n_key = n_seg * rows * cols
    q_flat = queries5.reshape(n_query, heads_local, head_size)
    keys = all_pair[..., :head_size].reshape(n_key, heads_local, head_size)
    values = all_pair[..., head_size:].reshape(n_key, heads_local, head_size)
    limit = valid_frames[0]
    keep = jnp.arange(n_key, dtype=jnp.int32) // (rows * cols) < limit
    scores = masked_scores(q_flat, keys, keep, scale)
    top = jnp.max(scores, axis=-1, keepdims=True)
    lse = top + jnp.log(jnp.sum(jnp.exp(scores - top), axis=-1, keepdims=True))
    prob = jnp.exp(scores - lse)
    prob_b = prob.astype(jnp.bfloat16)
    attn = jnp.einsum("hqk,khd->qhd", prob_b, values, preferred_element_type=jnp.float32).astype(
        jnp.bfloat16
    )
    grad = out_grad.reshape(n_query, heads_local, head_size)
    dprob = jnp.einsum("qhd,khd->hqk", grad, values, preferred_element_type=jnp.float32)
    delta = jnp.sum(grad.astype(jnp.float32) * attn.astype(jnp.float32), axis=-1).T
    dscore = (prob * (dprob - delta[:, :, None])).astype(jnp.bfloat16)
    q_grad = (
        jnp.einsum("hqk,khd->qhd", dscore, keys, preferred_element_type=jnp.float32) * scale
    ).astype(jnp.bfloat16)
    key_part = (
        jnp.einsum("hqk,qhd->khd", dscore, q_flat, preferred_element_type=jnp.float32) * scale
    ).astype(jnp.bfloat16)
    value_part = jnp.einsum(
        "hqk,qhd->khd", prob_b, grad, preferred_element_type=jnp.float32
    ).astype(jnp.bfloat16)
    kv_part = jnp.stack([key_part, value_part]).reshape(
        2, n_seg, 2, row_dev, cols, heads_local, head_size
    )
    kv_sum = kv_part[:, :, 0].astype(jnp.float32) + swap_seq(kv_part[:, :, 1]).astype(jnp.float32)
    kv_sum = kv_sum.astype(jnp.bfloat16)
    k_grad = kv_sum[0]
    v_grad = kv_sum[1]
    shape6 = (1, n_seg, row_dev, cols, heads_local, head_size)
    return (
        attn.reshape(shape6),
        q_grad.reshape(shape6),
        k_grad.reshape(shape6),
        v_grad.reshape(shape6),
    )


def inner_size(mesh):
    column = np.asarray(mesh.devices)[0, :, 0]
    try:
        count = len({d.coords[1] for d in column})
    except AttributeError:
        count = 1
    if count < 1 or column.size % count:
        count = 1
    return count


def solution(mesh):
    devices = np.asarray(mesh.devices)
    n_seg, n_mp, n_seq = devices.shape
    n_in = inner_size(mesh)
    split = Mesh(
        devices.reshape(n_seg, n_mp // n_in, n_in, n_seq), ("segment", OUTER, INNER, "seq")
    )
    placed = (
        P(MP, "segment", "seq", None, None),
        P(MP),
        P(MP),
        P(),
        P(None, "seq"),
        P("seq", "segment", None),
        P(MP, None, "seq", None, "segment", None),
    )
    out = P(MP, None, "seq", None, "segment", None)
    return jax.shard_map(
        on_device,
        mesh=split,
        in_specs=placed,
        out_specs=(out, out, out, out),
        check_vma=False,
    )
```
